1024 devices in a mesh: tm: 16 (over x, y), dp: 64 (over z, core).
Axes of the slice: x: 4, y: 4, z: 32, core: 2. Of those that a mesh axis runs over, the one named last changes fastest.
Arguments:
- video: bfloat16 [64, 16, 8, 24, 128], P('dp', 'tm'), may hold values from -17 to 17
- cotangent: bfloat16 [64, 16, 8, 24, 128], P('dp', 'tm'), may hold values from -6 to 6
- conv1_weight: bfloat16 [3456, 128], replicated, may hold values from -0.109375 to 0.109375
- conv2_weight: bfloat16 [3456, 128], replicated, may hold values from -0.109375 to 0.109375
Outputs:
- block_out: bfloat16 [64, 16, 8, 24, 128], P('dp', 'tm')
- grad_video: float32 [64, 16, 8, 24, 128], P('dp', 'tm')
- grad_conv1: float32 [3456, 128], P('dp', 'tm')
- grad_conv2: float32 [3456, 128], P('dp', 'tm')
The draws below stay inside these ranges and needn't reach their ends.
All inputs are finite; a program needn't handle non-finite values.
Results may differ from the reference program's by a relative error of at most 0.022.
Values may be sent and summed in bfloat16 or wider, within the bound.
No kernel may reach another device: no remote copies, remote signals or barrier semaphores. Data moves between devices by JAX's collectives and lax.ppermute only.
A program may use at most 64 MiB of HBM per device.

```python
import math
import jax
import jax.numpy as jnp
from jax import lax

C = 128
GROUPS = 32
HEIGHT = 8
WIDTH = 24
FRAMES = 16
CLIPS = 64


def draw_video(key, part):
    key_base, key_chan = jax.random.split(key, 2)
    position = jnp.arange(FRAMES, dtype=jnp.float32) / max(FRAMES - 1, 1)
    rising = (1.0 + 2.0 * position)[None, :, None, None, None]
    chan_scale = jnp.exp(jax.random.uniform(key_chan, (1, 1, 1, 1, C), jnp.float32, minval=math.log(0.3), maxval=math.log(3.0)))
    base = jax.random.truncated_normal(key_base, -4.0, 4.0, (CLIPS, FRAMES, HEIGHT, WIDTH, C), jnp.float32)
    values = 0.25 * base * rising * chan_scale
    return values.astype(jnp.bfloat16)


def draw_cotangent(key, part):
    key_noise, key_offset = jax.random.split(jax.random.fold_in(key, 7), 2)
    half_clips = CLIPS // 2
    shape = (CLIPS, FRAMES, HEIGHT, WIDTH, C)
    noise = jax.random.truncated_normal(key_noise, -4.0, 4.0, shape, jnp.float32)
    paired = jax.random.uniform(key_offset, (half_clips, 1, 1, 1, C), jnp.float32, minval=-2.0, maxval=2.0)
    offset = jnp.stack([paired, -paired], axis=1).reshape(CLIPS, 1, 1, 1, C)
    values = jnp.clip(noise + offset, -6.0, 6.0)
    return values.astype(jnp.bfloat16)


def bell_draw(key, dims, deviation, reach, held_as=jnp.bfloat16):
    drawn = jax.random.normal(key, dims, jnp.float32) * deviation
    return jnp.minimum(jnp.maximum(drawn, -reach), reach).astype(held_as)


def setup_inputs(seed: int = 0) -> dict:
    key_of = jax.random.split(jax.random.key(seed), 5)
    video = draw_video(jax.random.fold_in(key_of[4], 71), 0)
    cotangent = draw_cotangent(jax.random.fold_in(key_of[4], 71), 0)
    conv1_weight = bell_draw(key_of[2], (27 * C, C), (27 * C) ** -0.5, 0.109375)
    conv2_weight = bell_draw(key_of[3], (27 * C, C), (27 * C) ** -0.5, 0.109375)
    return dict(video=video, cotangent=cotangent, conv1_weight=conv1_weight, conv2_weight=conv2_weight)


EPSILON = 1e-06

def normalize(values):
    grouped = values.reshape(-1, GROUPS, C // GROUPS)
    average = lax.optimization_barrier(jnp.mean(grouped, axis=(0, 2)))
    centered = grouped - average[None, :, None]
    variance = lax.optimization_barrier(jnp.mean(centered * centered, axis=(0, 2)))
    inv_scale = lax.rsqrt(variance + EPSILON)
    return (centered * inv_scale[None, :, None], inv_scale)

def activate(normed):
    return (normed * jax.nn.sigmoid(normed)).astype(jnp.bfloat16)

def forward_patches(stacked):
    frames = stacked.shape[0] - 2
    padded = jnp.pad(stacked, ((0, 0), (1, 1), (1, 1), (0, 0)))
    columns = [padded[tap_t:tap_t + frames, tap_h:tap_h + HEIGHT, tap_w:tap_w + WIDTH, :] for tap_t in range(3) for tap_h in range(3) for tap_w in range(3)]
    return jnp.concatenate(columns, axis=-1).reshape(frames * HEIGHT * WIDTH, 27 * C)

def backward_patches(stacked):
    frames = stacked.shape[0] - 2
    padded = jnp.pad(stacked, ((0, 0), (1, 1), (1, 1), (0, 0)))
    columns = [padded[2 - tap_t:2 - tap_t + frames, 2 - tap_h:2 - tap_h + HEIGHT, 2 - tap_w:2 - tap_w + WIDTH, :] for tap_t in range(3) for tap_h in range(3) for tap_w in range(3)]
    return jnp.concatenate(columns, axis=-1).reshape(frames * HEIGHT * WIDTH, 27 * C)

def flipped(weight):
    return weight.reshape(27, C, C).transpose(0, 2, 1).reshape(27 * C, C)

def weight_grad(patches, grads):
    return lax.dot_general(patches, grads, (((0,), (0,)), ((), ())), preferred_element_type=jnp.float32)

def norm_backward(grad_act, normed, inv_scale):
    logistic = jax.nn.sigmoid(normed)
    grad_normed = grad_act * logistic * (1.0 + normed * (1.0 - logistic))
    first_mean = lax.optimization_barrier(jnp.mean(grad_normed, axis=(0, 2)))
    second_mean = lax.optimization_barrier(jnp.mean(grad_normed * normed, axis=(0, 2)))
    return inv_scale[None, :, None] * (grad_normed - first_mean[None, :, None] - normed * second_mean[None, :, None])

def reference(video, cotangent, conv1_weight, conv2_weight):
    leading_zeros = jnp.zeros((2, HEIGHT, WIDTH, C), jnp.bfloat16)
    flipped_one = flipped(conv1_weight)
    flipped_two = flipped(conv2_weight)

    def clip_step(totals, inputs):
        clip, grad_out = inputs
        layout = clip.shape
        first_normed, first_scale = normalize(clip.astype(jnp.float32))
        first_act = activate(first_normed).reshape(layout)
        first_patches = forward_patches(jnp.concatenate([leading_zeros, first_act], axis=0))
        hidden = jnp.dot(first_patches, conv1_weight, preferred_element_type=jnp.float32).astype(jnp.bfloat16).reshape(layout)
        second_normed, second_scale = normalize(hidden.astype(jnp.float32))
        second_act = activate(second_normed).reshape(layout)
        second_patches = forward_patches(jnp.concatenate([leading_zeros, second_act], axis=0))
        mixed = jnp.dot(second_patches, conv2_weight, preferred_element_type=jnp.float32).reshape(layout)
        block_out = (clip.astype(jnp.float32) + mixed).astype(jnp.bfloat16)
        grad_w2 = weight_grad(second_patches, grad_out.reshape(-1, C))
        grad_second = jnp.dot(backward_patches(jnp.concatenate([grad_out, leading_zeros], axis=0)), flipped_two, preferred_element_type=jnp.float32)
        grad_hidden = norm_backward(grad_second.reshape(-1, GROUPS, C // GROUPS), second_normed, second_scale)
        grad_hidden = grad_hidden.astype(jnp.bfloat16).reshape(layout)
        grad_w1 = weight_grad(first_patches, grad_hidden.reshape(-1, C))
        grad_first = jnp.dot(backward_patches(jnp.concatenate([grad_hidden, leading_zeros], axis=0)), flipped_one, preferred_element_type=jnp.float32)
        grad_video = grad_out.astype(jnp.float32) + norm_backward(grad_first.reshape(-1, GROUPS, C // GROUPS), first_normed, first_scale).reshape(layout)
        return ((totals[0] + grad_w1, totals[1] + grad_w2), (block_out, grad_video))
    start = (jnp.zeros((27 * C, C), jnp.float32), jnp.zeros((27 * C, C), jnp.float32))
    totals, outputs = lax.scan(clip_step, start, (video, cotangent))
    factor = 1.0 / math.sqrt(CLIPS * FRAMES * HEIGHT * WIDTH)
    return (outputs[0], outputs[1], totals[0] * factor, totals[1] * factor)
```

```python
import math

import jax
import jax.numpy as jnp
from jax import lax
from jax.sharding import PartitionSpec as P

GROUPS = 32


EPSILON = 1e-06

FORWARD_DIMS = ("NDHWC", "DHWIO", "NDHWC")
TRANSPOSED_DIMS = ("NDHWC", "DHWOI", "NDHWC")
WEIGHT_DIMS = ("CDHWN", "IDHWO", "NDHWC")


def normalize(values):
    grouped = values.reshape(-1, GROUPS, values.shape[-1] // GROUPS)
    average = jnp.mean(grouped, axis=(0, 2))
    centered = grouped - average[None, :, None]
    variance = jnp.mean(centered * centered, axis=(0, 2))
    inv_scale = lax.rsqrt(variance + EPSILON)
    return (centered * inv_scale[None, :, None], inv_scale)


def norm_backward(grad_act, normed, inv_scale):
    logistic = jax.nn.sigmoid(normed)
    grad_normed = grad_act * logistic * (1.0 + normed * (1.0 - logistic))
    first_mean = jnp.mean(grad_normed, axis=(0, 2))
    second_mean = jnp.mean(grad_normed * normed, axis=(0, 2))
    return inv_scale[None, :, None] * (
        grad_normed - first_mean[None, :, None] - normed * second_mean[None, :, None]
    )


def kernel_of(weight):
    chans = weight.shape[1]
    return weight.reshape(3, 3, 3, weight.shape[0] // (27), chans)


def conv_clip(act, weight):
    out = lax.conv_general_dilated(
        act[None],
        kernel_of(weight),
        window_strides=(1, 1, 1),
        padding=((2, 0), (1, 1), (1, 1)),
        dimension_numbers=FORWARD_DIMS,
        preferred_element_type=jnp.float32,
    )
    return out[0]


def conv_window(window, weight):
    out = lax.conv_general_dilated(
        window[None],
        kernel_of(weight),
        window_strides=(1, 1, 1),
        padding=((0, 0), (1, 1), (1, 1)),
        dimension_numbers=FORWARD_DIMS,
        preferred_element_type=jnp.float32,
    )
    return out[0]


def conv_transposed(grad, weight):
    kernel = kernel_of(weight)[::-1, ::-1, ::-1]
    out = lax.conv_general_dilated(
        grad[None],
        kernel,
        window_strides=(1, 1, 1),
        padding=((0, 2), (1, 1), (1, 1)),
        dimension_numbers=TRANSPOSED_DIMS,
        preferred_element_type=jnp.float32,
    )
    return out[0]


def weight_grad(act, grad):
    padded = jnp.pad(act, ((2, 0), (1, 1), (1, 1), (0, 0)))
    out = lax.conv_general_dilated(
        padded[None],
        grad[None],
        window_strides=(1, 1, 1),
        padding="VALID",
        dimension_numbers=WEIGHT_DIMS,
        preferred_element_type=jnp.float32,
    )
    chans_in = act.shape[-1]
    return out.transpose(1, 2, 3, 0, 4).reshape(27 * chans_in, grad.shape[-1])


def body(video, cotangent, conv1_weight, conv2_weight):
    own_frame = video[0]
    grad_own = cotangent[0]
    layout = own_frame.shape
    height, width, chans = (layout[1], layout[2], layout[3])
    frames = lax.axis_size("tm")
    me = lax.axis_index("tm")
    cols = chans // frames
    grouping = (-1, GROUPS, chans // GROUPS)

    both = jnp.concatenate([own_frame, grad_own], axis=0)
    gathered = lax.all_gather(both, "tm", axis=0, tiled=False)
    clip = gathered[:, 0]
    grad_out = gathered[:, 1]
    clip_layout = clip.shape

    first_normed, first_scale = normalize(clip.astype(jnp.float32))
    first_act = (first_normed * jax.nn.sigmoid(first_normed)).astype(jnp.bfloat16).reshape(clip_layout)
    hidden = conv_clip(first_act, conv1_weight).astype(jnp.bfloat16)
    second_normed, second_scale = normalize(hidden.astype(jnp.float32))
    second_act = (
        (second_normed * jax.nn.sigmoid(second_normed)).astype(jnp.bfloat16).reshape(clip_layout)
    )
    second_padded = jnp.pad(second_act, ((2, 0), (0, 0), (0, 0), (0, 0)))
    window = lax.dynamic_slice_in_dim(second_padded, me, 3, axis=0)
    mixed = conv_window(window, conv2_weight)
    block_out = (own_frame.astype(jnp.float32) + mixed).astype(jnp.bfloat16)

    grad_second = conv_transposed(grad_out, conv2_weight)
    grad_hidden = norm_backward(grad_second.reshape(grouping), second_normed, second_scale)
    grad_hidden = grad_hidden.astype(jnp.bfloat16).reshape(clip_layout)
    grad_first = conv_transposed(grad_hidden, conv1_weight)
    grad_first_act = norm_backward(grad_first.reshape(grouping), first_normed, first_scale)
    grad_first_act = grad_first_act.reshape(clip_layout)
    grad_video = grad_own.astype(jnp.float32) + lax.dynamic_slice_in_dim(grad_first_act, me, 1, axis=0)

    my_cols = lambda values: lax.dynamic_slice_in_dim(values, me * cols, cols, axis=3)
    grad_w2 = weight_grad(second_act, my_cols(grad_out))
    grad_w1 = weight_grad(first_act, my_cols(grad_hidden))
    stacked = jnp.stack([grad_w1.reshape(-1), grad_w2.reshape(-1)])
    reduced = lax.psum_scatter(stacked, "dp", scatter_dimension=1, tiled=True)
    rows = grad_w1.shape[0] // lax.axis_size("dp")
    factor = 1.0 / math.sqrt(frames * lax.axis_size("dp") * height * width)
    total_w1 = reduced[0].reshape(rows, cols) * factor
    total_w2 = reduced[1].reshape(rows, cols) * factor
    return (block_out[None], grad_video[None], total_w1, total_w2)


def solution(mesh):
    placed = (P("dp", "tm", None, None, None), P("dp", "tm", None, None, None), P(), P())
    return jax.shard_map(
        body,
        mesh=mesh,
        in_specs=placed,
        out_specs=(
            P("dp", "tm", None, None, None),
            P("dp", "tm", None, None, None),
            P("dp", "tm"),
            P("dp", "tm"),
        ),
        check_vma=False,
    )
```

```python
import math

import jax
import jax.numpy as jnp
from jax import lax
from jax.sharding import PartitionSpec as P

GROUPS = 32


EPSILON = 1e-06

FORWARD_DIMS = ("NDHWC", "DHWIO", "NDHWC")
TRANSPOSED_DIMS = ("NDHWC", "DHWOI", "NDHWC")
WEIGHT_DIMS = ("CDHWN", "IDHWO", "NDHWC")


def normalize(values):
    grouped = values.reshape(-1, GROUPS, values.shape[-1] // GROUPS)
    average = jnp.mean(grouped, axis=(0, 2))
    centered = grouped - average[None, :, None]
    variance = jnp.mean(centered * centered, axis=(0, 2))
    inv_scale = lax.rsqrt(variance + EPSILON)
    return (centered * inv_scale[None, :, None], inv_scale)


def norm_backward(grad_act, normed, inv_scale):
    logistic = jax.nn.sigmoid(normed)
    grad_normed = grad_act * logistic * (1.0 + normed * (1.0 - logistic))
    first_mean = jnp.mean(grad_normed, axis=(0, 2))
    second_mean = jnp.mean(grad_normed * normed, axis=(0, 2))
    return inv_scale[None, :, None] * (
        grad_normed - first_mean[None, :, None] - normed * second_mean[None, :, None]
    )


def kernel_of(weight):
    chans = weight.shape[1]
    return weight.reshape(3, 3, 3, weight.shape[0] // (27), chans)


def conv_clip(act, weight):
    out = lax.conv_general_dilated(
        act[None],
        kernel_of(weight),
        window_strides=(1, 1, 1),
        padding=((2, 0), (1, 1), (1, 1)),
        dimension_numbers=FORWARD_DIMS,
        preferred_element_type=jnp.float32,
    )
    return out[0]


def conv_window(window, weight):
    out = lax.conv_general_dilated(
        window[None],
        kernel_of(weight),
        window_strides=(1, 1, 1),
        padding=((0, 0), (1, 1), (1, 1)),
        dimension_numbers=FORWARD_DIMS,
        preferred_element_type=jnp.float32,
    )
    return out[0]


def conv_transposed(grad, weight):
    kernel = kernel_of(weight)[::-1, ::-1, ::-1]
    out = lax.conv_general_dilated(
        grad[None],
        kernel,
        window_strides=(1, 1, 1),
        padding=((0, 2), (1, 1), (1, 1)),
        dimension_numbers=TRANSPOSED_DIMS,
        preferred_element_type=jnp.float32,
    )
    return out[0]


def weight_grad(act, grad):
    padded = jnp.pad(act, ((2, 0), (1, 1), (1, 1), (0, 0)))
    grid = padded.shape[:3]
    positions = grid[0] * grid[1] * grid[2]
    chans_in = act.shape[-1]
    cols = grad.shape[-1]
    placed = jnp.pad(
        grad.transpose(3, 0, 1, 2),
        ((0, 0), (0, grid[0] - grad.shape[0]), (0, grid[1] - grad.shape[1]), (0, grid[2] - grad.shape[2])),
    ).reshape(cols, positions)
    plane, row = grid[1] * grid[2], grid[2]
    offsets = [t * plane + r * row + s for t in range(3) for r in range(3) for s in range(3)]
    lead = max(offsets)
    prefixed = jnp.pad(placed, ((0, 0), (lead, 0)))
    taps = jnp.concatenate([prefixed[:, lead - o : lead - o + positions] for o in offsets], axis=0)
    out = lax.dot_general(
        taps,
        padded.reshape(positions, chans_in),
        (((1,), (0,)), ((), ())),
        preferred_element_type=jnp.float32,
    )
    return out.reshape(27, cols, chans_in).transpose(0, 2, 1).reshape(27 * chans_in, cols)


def gather_frames(block, axis, order):
    me = lax.axis_index(axis)
    size = lax.axis_size(axis)
    held = block
    for bit in order:
        step = 1 << bit
        arrived = lax.ppermute(held, axis, [(i, i ^ step) for i in range(size)])
        upper = (me >> bit) & 1
        held = jnp.where(upper == 1, jnp.stack([arrived, held]), jnp.stack([held, arrived]))
    last_first = list(reversed(order))
    natural = sorted(range(len(order)), key=lambda k: -last_first[k])
    held = held.transpose(natural + list(range(len(order), held.ndim)))
    return held.reshape((size,) + block.shape)


def reduce_blocks(blocks, axis):
    me = lax.axis_index(axis)
    size = lax.axis_size(axis)
    held = blocks
    bit = 0
    while (1 << bit) < size:
        pairs = held.reshape(held.shape[0] // 2, 2, held.shape[1])
        mine = (me >> bit) & 1
        keep = lax.dynamic_index_in_dim(pairs, mine, axis=1, keepdims=False)
        send = lax.dynamic_index_in_dim(pairs, 1 - mine, axis=1, keepdims=False)
        step = 1 << bit
        arrived = lax.ppermute(send, axis, [(i, i ^ step) for i in range(size)])
        held = keep + arrived
        bit += 1
    return held[0]


def bit_order(size):
    bits = list(range(size.bit_length() - 1))
    return [b for b in bits if b % 2 == 1] + [b for b in bits if b % 2 == 0]


def body(video, cotangent, conv1_weight, conv2_weight):
    own_frame = video[0]
    grad_own = cotangent[0]
    layout = own_frame.shape
    height, width_px, chans = (layout[1], layout[2], layout[3])
    frames = lax.axis_size("tm")
    me = lax.axis_index("tm")
    cols = chans // frames
    grouping = (-1, GROUPS, chans // GROUPS)

    order = bit_order(frames)
    clip = gather_frames(own_frame[0], "tm", order)
    grad_out = gather_frames(grad_own[0], "tm", order)
    clip_layout = clip.shape

    first_normed, first_scale = normalize(clip.astype(jnp.float32))
    first_act = (first_normed * jax.nn.sigmoid(first_normed)).astype(jnp.bfloat16).reshape(clip_layout)
    hidden = conv_clip(first_act, conv1_weight).astype(jnp.bfloat16)
    second_normed, second_scale = normalize(hidden.astype(jnp.float32))
    second_act = (
        (second_normed * jax.nn.sigmoid(second_normed)).astype(jnp.bfloat16).reshape(clip_layout)
    )
    second_padded = jnp.pad(second_act, ((2, 0), (0, 0), (0, 0), (0, 0)))
    window = lax.dynamic_slice_in_dim(second_padded, me, 3, axis=0)
    mixed = conv_window(window, conv2_weight)
    block_out = (own_frame.astype(jnp.float32) + mixed).astype(jnp.bfloat16)

    grad_second = conv_transposed(grad_out, conv2_weight)
    grad_hidden = norm_backward(grad_second.reshape(grouping), second_normed, second_scale)
    grad_hidden = grad_hidden.astype(jnp.bfloat16).reshape(clip_layout)
    grad_first = conv_transposed(grad_hidden, conv1_weight)
    grad_first_act = norm_backward(grad_first.reshape(grouping), first_normed, first_scale)
    grad_first_act = grad_first_act.reshape(clip_layout)
    grad_video = grad_own.astype(jnp.float32) + lax.dynamic_slice_in_dim(grad_first_act, me, 1, axis=0)

    my_cols = lambda values: lax.dynamic_slice_in_dim(values, me * cols, cols, axis=3)
    grad_w2 = weight_grad(second_act, my_cols(grad_out))
    grad_w1 = weight_grad(first_act, my_cols(grad_hidden))
    parts = lax.axis_size("dp")
    rows = grad_w1.shape[0] // parts
    share = rows * cols
    width = -(-2 * share // 1024) * 1024
    blocks = jnp.concatenate(
        [
            grad_w1.reshape(parts, share),
            grad_w2.reshape(parts, share),
            jnp.zeros((parts, width - 2 * share), jnp.float32),
        ],
        axis=1,
    )
    reduced = reduce_blocks(blocks, "dp")
    factor = 1.0 / math.sqrt(frames * parts * height * width_px)
    total_w1 = reduced[:share].reshape(rows, cols) * factor
    total_w2 = reduced[share : 2 * share].reshape(rows, cols) * factor
    return (block_out[None], grad_video[None], total_w1, total_w2)


def solution(mesh):
    placed = (P("dp", "tm", None, None, None), P("dp", "tm", None, None, None), P(), P())
    return jax.shard_map(
        body,
        mesh=mesh,
        in_specs=placed,
        out_specs=(
            P("dp", "tm", None, None, None),
            P("dp", "tm", None, None, None),
            P("dp", "tm"),
            P("dp", "tm"),
        ),
        check_vma=False,
    )
```

```python
import math

import jax
import jax.numpy as jnp
from jax import lax
from jax.sharding import PartitionSpec as P

GROUPS = 32


EPSILON = 1e-06

FORWARD_DIMS = ("NDHWC", "DHWIO", "NDHWC")
TRANSPOSED_DIMS = ("NDHWC", "DHWOI", "NDHWC")
WEIGHT_DIMS = ("CDHWN", "IDHWO", "NDHWC")


def normalize(values):
    grouped = values.reshape(-1, GROUPS, values.shape[-1] // GROUPS)
    average = jnp.mean(grouped, axis=(0, 2))
    centered = grouped - average[None, :, None]
    variance = jnp.mean(centered * centered, axis=(0, 2))
    inv_scale = lax.rsqrt(variance + EPSILON)
    return (centered * inv_scale[None, :, None], inv_scale)


def norm_backward(grad_act, normed, inv_scale):
    logistic = jax.nn.sigmoid(normed)
    grad_normed = grad_act * logistic * (1.0 + normed * (1.0 - logistic))
    first_mean = jnp.mean(grad_normed, axis=(0, 2))
    second_mean = jnp.mean(grad_normed * normed, axis=(0, 2))
    return inv_scale[None, :, None] * (
        grad_normed - first_mean[None, :, None] - normed * second_mean[None, :, None]
    )


def kernel_of(weight):
    chans = weight.shape[1]
    return weight.reshape(3, 3, 3, weight.shape[0] // (27), chans)


def conv_clip(act, weight):
    out = lax.conv_general_dilated(
        act[None],
        kernel_of(weight),
        window_strides=(1, 1, 1),
        padding=((2, 0), (1, 1), (1, 1)),
        dimension_numbers=FORWARD_DIMS,
        preferred_element_type=jnp.float32,
    )
    return out[0]


def conv_window(window, weight):
    out = lax.conv_general_dilated(
        window[None],
        kernel_of(weight),
        window_strides=(1, 1, 1),
        padding=((0, 0), (1, 1), (1, 1)),
        dimension_numbers=FORWARD_DIMS,
        preferred_element_type=jnp.float32,
    )
    return out[0]


def conv_transposed(grad, weight):
    kernel = kernel_of(weight)[::-1, ::-1, ::-1]
    out = lax.conv_general_dilated(
        grad[None],
        kernel,
        window_strides=(1, 1, 1),
        padding=((0, 2), (1, 1), (1, 1)),
        dimension_numbers=TRANSPOSED_DIMS,
        preferred_element_type=jnp.float32,
    )
    return out[0]


def weight_grad(act, grad):
    padded = jnp.pad(act, ((2, 0), (1, 1), (1, 1), (0, 0)))
    grid = padded.shape[:3]
    positions = grid[0] * grid[1] * grid[2]
    chans_in = act.shape[-1]
    cols = grad.shape[-1]
    placed = jnp.pad(
        grad.transpose(3, 0, 1, 2),
        ((0, 0), (0, grid[0] - grad.shape[0]), (0, grid[1] - grad.shape[1]), (0, grid[2] - grad.shape[2])),
    ).reshape(cols, positions)
    plane, row = grid[1] * grid[2], grid[2]
    offsets = [t * plane + r * row + s for t in range(3) for r in range(3) for s in range(3)]
    lead = max(offsets)
    prefixed = jnp.pad(placed, ((0, 0), (lead, 0)))
    taps = jnp.concatenate([prefixed[:, lead - o : lead - o + positions] for o in offsets], axis=0)
    out = lax.dot_general(
        taps,
        padded.reshape(positions, chans_in),
        (((1,), (0,)), ((), ())),
        preferred_element_type=jnp.float32,
    )
    return out.reshape(27, cols, chans_in).transpose(0, 2, 1).reshape(27 * chans_in, cols)


def digits_of(size, radices):
    out, weight = [], 1
    for radix in radices:
        out.append((weight, radix))
        weight *= radix
    assert weight == size
    return out


def gather_frames(block, axis, radices):
    me = lax.axis_index(axis)
    size = lax.axis_size(axis)
    held = block[None]
    for weight, radix in digits_of(size, radices):
        options = [held] + [
            lax.ppermute(held, axis, [(i, i ^ (k * weight)) for i in range(size)])
            for k in range(1, radix)
        ]
        options = jnp.stack(options)
        digit = (me // weight) % radix
        held = jnp.concatenate(
            [lax.dynamic_index_in_dim(options, digit ^ v, axis=0, keepdims=False) for v in range(radix)],
            axis=0,
        )
    return held.reshape((size,) + block.shape)


def reduce_blocks(blocks, axis, radices):
    me = lax.axis_index(axis)
    size = lax.axis_size(axis)
    held = blocks
    for weight, radix in digits_of(size, radices):
        grouped = held.reshape(held.shape[0] // radix, radix, held.shape[1])
        digit = (me // weight) % radix
        total = lax.dynamic_index_in_dim(grouped, digit, axis=1, keepdims=False)
        for k in range(1, radix):
            send = lax.dynamic_index_in_dim(grouped, digit ^ k, axis=1, keepdims=False)
            total = total + lax.ppermute(send, axis, [(i, i ^ (k * weight)) for i in range(size)])
        held = total
    return held[0]


def radices_of(size, first):
    out, rest = [], size
    for radix in first:
        if radix > 1 and rest % radix == 0:
            out.append(radix)
            rest //= radix
    while rest > 1:
        out.append(2)
        rest //= 2
    return out


def body(video, cotangent, conv1_weight, conv2_weight):
    own_frame = video[0]
    grad_own = cotangent[0]
    layout = own_frame.shape
    height, width_px, chans = (layout[1], layout[2], layout[3])
    frames = lax.axis_size("tm")
    me = lax.axis_index("tm")
    cols = chans // frames
    grouping = (-1, GROUPS, chans // GROUPS)

    frame_radices = radices_of(frames, (4, 4))
    clip = gather_frames(own_frame[0], "tm", frame_radices)
    grad_out = gather_frames(grad_own[0], "tm", frame_radices)
    clip_layout = clip.shape

    first_normed, first_scale = normalize(clip.astype(jnp.float32))
    first_act = (first_normed * jax.nn.sigmoid(first_normed)).astype(jnp.bfloat16).reshape(clip_layout)
    hidden = conv_clip(first_act, conv1_weight).astype(jnp.bfloat16)
    second_normed, second_scale = normalize(hidden.astype(jnp.float32))
    second_act = (
        (second_normed * jax.nn.sigmoid(second_normed)).astype(jnp.bfloat16).reshape(clip_layout)
    )
    second_padded = jnp.pad(second_act, ((2, 0), (0, 0), (0, 0), (0, 0)))
    window = lax.dynamic_slice_in_dim(second_padded, me, 3, axis=0)
    mixed = conv_window(window, conv2_weight)
    block_out = (own_frame.astype(jnp.float32) + mixed).astype(jnp.bfloat16)

    grad_second = conv_transposed(grad_out, conv2_weight)
    grad_hidden = norm_backward(grad_second.reshape(grouping), second_normed, second_scale)
    grad_hidden = grad_hidden.astype(jnp.bfloat16).reshape(clip_layout)
    grad_first = conv_transposed(grad_hidden, conv1_weight)
    grad_first_act = norm_backward(grad_first.reshape(grouping), first_normed, first_scale)
    grad_first_act = grad_first_act.reshape(clip_layout)
    grad_video = grad_own.astype(jnp.float32) + lax.dynamic_slice_in_dim(grad_first_act, me, 1, axis=0)

    my_cols = lambda values: lax.dynamic_slice_in_dim(values, me * cols, cols, axis=3)
    grad_w2 = weight_grad(second_act, my_cols(grad_out))
    grad_w1 = weight_grad(first_act, my_cols(grad_hidden))
    parts = lax.axis_size("dp")
    rows = grad_w1.shape[0] // parts
    share = rows * cols
    width = -(-2 * share // 1024) * 1024
    blocks = jnp.concatenate(
        [
            grad_w1.reshape(parts, share),
            grad_w2.reshape(parts, share),
            jnp.zeros((parts, width - 2 * share), jnp.float32),
        ],
        axis=1,
    )
    reduced = reduce_blocks(blocks, "dp", radices_of(parts, (2, 4, parts // 8)))
    factor = 1.0 / math.sqrt(frames * parts * height * width_px)
    total_w1 = reduced[:share].reshape(rows, cols) * factor
    total_w2 = reduced[share : 2 * share].reshape(rows, cols) * factor
    return (block_out[None], grad_video[None], total_w1, total_w2)


def solution(mesh):
    placed = (P("dp", "tm", None, None, None), P("dp", "tm", None, None, None), P(), P())
    return jax.shard_map(
        body,
        mesh=mesh,
        in_specs=placed,
        out_specs=(
            P("dp", "tm", None, None, None),
            P("dp", "tm", None, None, None),
            P("dp", "tm"),
            P("dp", "tm"),
        ),
        check_vma=False,
    )
```

```python
import math

import jax
import jax.numpy as jnp
from jax import lax
from jax.sharding import PartitionSpec as P

GROUPS = 32


EPSILON = 1e-06

FORWARD_DIMS = ("NDHWC", "DHWIO", "NDHWC")
TRANSPOSED_DIMS = ("NDHWC", "DHWOI", "NDHWC")
WEIGHT_DIMS = ("CDHWN", "IDHWO", "NDHWC")


def normalize(values):
    grouped = values.reshape(-1, GROUPS, values.shape[-1] // GROUPS)
    average = jnp.mean(grouped, axis=(0, 2))
    centered = grouped - average[None, :, None]
    variance = jnp.mean(centered * centered, axis=(0, 2))
    inv_scale = lax.rsqrt(variance + EPSILON)
    return (centered * inv_scale[None, :, None], inv_scale)


def norm_backward(grad_act, normed, inv_scale):
    logistic = jax.nn.sigmoid(normed)
    grad_normed = grad_act * logistic * (1.0 + normed * (1.0 - logistic))
    first_mean = jnp.mean(grad_normed, axis=(0, 2))
    second_mean = jnp.mean(grad_normed * normed, axis=(0, 2))
    return inv_scale[None, :, None] * (
        grad_normed - first_mean[None, :, None] - normed * second_mean[None, :, None]
    )


def kernel_of(weight):
    chans = weight.shape[1]
    return weight.reshape(3, 3, 3, weight.shape[0] // (27), chans)


def conv_clip(act, weight):
    out = lax.conv_general_dilated(
        act[None],
        kernel_of(weight),
        window_strides=(1, 1, 1),
        padding=((2, 0), (1, 1), (1, 1)),
        dimension_numbers=FORWARD_DIMS,
        preferred_element_type=jnp.float32,
    )
    return out[0]


def conv_window(window, weight):
    out = lax.conv_general_dilated(
        window[None],
        kernel_of(weight),
        window_strides=(1, 1, 1),
        padding=((0, 0), (1, 1), (1, 1)),
        dimension_numbers=FORWARD_DIMS,
        preferred_element_type=jnp.float32,
    )
    return out[0]


def conv_transposed(grad, weight):
    kernel = kernel_of(weight)[::-1, ::-1, ::-1]
    out = lax.conv_general_dilated(
        grad[None],
        kernel,
        window_strides=(1, 1, 1),
        padding=((0, 2), (1, 1), (1, 1)),
        dimension_numbers=TRANSPOSED_DIMS,
        preferred_element_type=jnp.float32,
    )
    return out[0]


def weight_grad(act, grad):
    padded = jnp.pad(act, ((2, 0), (1, 1), (1, 1), (0, 0)))
    grid = padded.shape[:3]
    positions = grid[0] * grid[1] * grid[2]
    chans_in = act.shape[-1]
    cols = grad.shape[-1]
    placed = jnp.pad(
        grad.transpose(3, 0, 1, 2),
        ((0, 0), (0, grid[0] - grad.shape[0]), (0, grid[1] - grad.shape[1]), (0, grid[2] - grad.shape[2])),
    ).reshape(cols, positions)
    plane, row = grid[1] * grid[2], grid[2]
    offsets = [t * plane + r * row + s for t in range(3) for r in range(3) for s in range(3)]
    lead = max(offsets)
    prefixed = jnp.pad(placed, ((0, 0), (lead, 0)))
    taps = jnp.concatenate([prefixed[:, lead - o : lead - o + positions] for o in offsets], axis=0)
    out = lax.dot_general(
        taps,
        padded.reshape(positions, chans_in),
        (((1,), (0,)), ((), ())),
        preferred_element_type=jnp.float32,
    )
    return out.reshape(27, cols, chans_in).transpose(0, 2, 1).reshape(27 * chans_in, cols)


def digits_of(size, radices):
    out, weight = [], 1
    for radix in radices:
        out.append((weight, radix))
        weight *= radix
    assert weight == size
    return out


def gather_frames(block, axis, order):
    me = lax.axis_index(axis)
    size = lax.axis_size(axis)
    held = block
    for bit in order:
        step = 1 << bit
        arrived = lax.ppermute(held, axis, [(i, i ^ step) for i in range(size)])
        upper = (me >> bit) & 1
        held = jnp.where(upper == 1, jnp.stack([arrived, held]), jnp.stack([held, arrived]))
    last_first = list(reversed(order))
    natural = sorted(range(len(order)), key=lambda k: -last_first[k])
    held = held.transpose(natural + list(range(len(order), held.ndim)))
    return held.reshape((size,) + block.shape)


def bit_order(size):
    bits = list(range(size.bit_length() - 1))
    return [b for b in bits if b % 2 == 1] + [b for b in bits if b % 2 == 0]


def reduce_blocks(blocks, axis, radices):
    me = lax.axis_index(axis)
    size = lax.axis_size(axis)
    held = blocks
    for weight, radix in digits_of(size, radices):
        grouped = held.reshape(held.shape[0] // radix, radix, held.shape[1])
        digit = (me // weight) % radix
        total = lax.dynamic_index_in_dim(grouped, digit, axis=1, keepdims=False)
        for k in range(1, radix):
            send = lax.dynamic_index_in_dim(grouped, digit ^ k, axis=1, keepdims=False)
            total = total + lax.ppermute(send, axis, [(i, i ^ (k * weight)) for i in range(size)])
        held = total
    return held[0]


def radices_of(size, first):
    out, rest = [], size
    for radix in first:
        if radix > 1 and rest % radix == 0:
            out.append(radix)
            rest //= radix
    while rest > 1:
        out.append(2)
        rest //= 2
    return out


def body(video, cotangent, conv1_weight, conv2_weight):
    own_frame = video[0]
    grad_own = cotangent[0]
    layout = own_frame.shape
    height, width_px, chans = (layout[1], layout[2], layout[3])
    frames = lax.axis_size("tm")
    me = lax.axis_index("tm")
    cols = chans // frames
    grouping = (-1, GROUPS, chans // GROUPS)

    both = jnp.stack([own_frame[0], grad_own[0]])
    gathered = gather_frames(both, "tm", bit_order(frames))
    clip = gathered[:, 0]
    grad_out = gathered[:, 1]
    clip_layout = clip.shape

    first_normed, first_scale = normalize(clip.astype(jnp.float32))
    first_act = (first_normed * jax.nn.sigmoid(first_normed)).astype(jnp.bfloat16).reshape(clip_layout)
    hidden = conv_clip(first_act, conv1_weight).astype(jnp.bfloat16)
    second_normed, second_scale = normalize(hidden.astype(jnp.float32))
    second_act = (
        (second_normed * jax.nn.sigmoid(second_normed)).astype(jnp.bfloat16).reshape(clip_layout)
    )
    second_padded = jnp.pad(second_act, ((2, 0), (0, 0), (0, 0), (0, 0)))
    window = lax.dynamic_slice_in_dim(second_padded, me, 3, axis=0)
    mixed = conv_window(window, conv2_weight)
    block_out = (own_frame.astype(jnp.float32) + mixed).astype(jnp.bfloat16)

    grad_second = conv_transposed(grad_out, conv2_weight)
    grad_hidden = norm_backward(grad_second.reshape(grouping), second_normed, second_scale)
    grad_hidden = grad_hidden.astype(jnp.bfloat16).reshape(clip_layout)
    grad_first = conv_transposed(grad_hidden, conv1_weight)
    grad_first_act = norm_backward(grad_first.reshape(grouping), first_normed, first_scale)
    grad_first_act = grad_first_act.reshape(clip_layout)
    grad_video = grad_own.astype(jnp.float32) + lax.dynamic_slice_in_dim(grad_first_act, me, 1, axis=0)

    my_cols = lambda values: lax.dynamic_slice_in_dim(values, me * cols, cols, axis=3)
    grad_w2 = weight_grad(second_act, my_cols(grad_out))
    grad_w1 = weight_grad(first_act, my_cols(grad_hidden))
    parts = lax.axis_size("dp")
    rows = grad_w1.shape[0] // parts
    share = rows * cols
    width = -(-2 * share // 1024) * 1024
    blocks = jnp.concatenate(
        [
            grad_w1.reshape(parts, share),
            grad_w2.reshape(parts, share),
            jnp.zeros((parts, width - 2 * share), jnp.float32),
        ],
        axis=1,
    )
    reduced = reduce_blocks(blocks, "dp", radices_of(parts, ()))
    factor = 1.0 / math.sqrt(frames * parts * height * width_px)
    total_w1 = reduced[:share].reshape(rows, cols) * factor
    total_w2 = reduced[share : 2 * share].reshape(rows, cols) * factor
    return (block_out[None], grad_video[None], total_w1, total_w2)


def solution(mesh):
    placed = (P("dp", "tm", None, None, None), P("dp", "tm", None, None, None), P(), P())
    return jax.shard_map(
        body,
        mesh=mesh,
        in_specs=placed,
        out_specs=(
            P("dp", "tm", None, None, None),
            P("dp", "tm", None, None, None),
            P("dp", "tm"),
            P("dp", "tm"),
        ),
        check_vma=False,
    )
```

```python
import math

import jax
import jax.numpy as jnp
from jax import lax
from jax.sharding import PartitionSpec as P

GROUPS = 32


EPSILON = 1e-06

FORWARD_DIMS = ("NDHWC", "DHWIO", "NDHWC")
TRANSPOSED_DIMS = ("NDHWC", "DHWOI", "NDHWC")
WEIGHT_DIMS = ("CDHWN", "IDHWO", "NDHWC")


def normalize(values):
    grouped = values.reshape(-1, GROUPS, values.shape[-1] // GROUPS)
    average = jnp.mean(grouped, axis=(0, 2))
    centered = grouped - average[None, :, None]
    variance = jnp.mean(centered * centered, axis=(0, 2))
    inv_scale = lax.rsqrt(variance + EPSILON)
    return (centered * inv_scale[None, :, None], inv_scale)


def norm_backward(grad_act, normed, inv_scale):
    logistic = jax.nn.sigmoid(normed)
    grad_normed = grad_act * logistic * (1.0 + normed * (1.0 - logistic))
    first_mean = jnp.mean(grad_normed, axis=(0, 2))
    second_mean = jnp.mean(grad_normed * normed, axis=(0, 2))
    return inv_scale[None, :, None] * (
        grad_normed - first_mean[None, :, None] - normed * second_mean[None, :, None]
    )


def kernel_of(weight):
    chans = weight.shape[1]
    return weight.reshape(3, 3, 3, weight.shape[0] // (27), chans)


def conv_clip(act, weight):
    out = lax.conv_general_dilated(
        act[None],
        kernel_of(weight),
        window_strides=(1, 1, 1),
        padding=((2, 0), (1, 1), (1, 1)),
        dimension_numbers=FORWARD_DIMS,
        preferred_element_type=jnp.float32,
    )
    return out[0]


def conv_window(window, weight):
    out = lax.conv_general_dilated(
        window[None],
        kernel_of(weight),
        window_strides=(1, 1, 1),
        padding=((0, 0), (1, 1), (1, 1)),
        dimension_numbers=FORWARD_DIMS,
        preferred_element_type=jnp.float32,
    )
    return out[0]


def conv_transposed(grad, weight):
    kernel = kernel_of(weight)[::-1, ::-1, ::-1]
    out = lax.conv_general_dilated(
        grad[None],
        kernel,
        window_strides=(1, 1, 1),
        padding=((0, 2), (1, 1), (1, 1)),
        dimension_numbers=TRANSPOSED_DIMS,
        preferred_element_type=jnp.float32,
    )
    return out[0]


def weight_grad(act, grad):
    padded = jnp.pad(act, ((2, 0), (1, 1), (1, 1), (0, 0)))
    grid = padded.shape[:3]
    positions = grid[0] * grid[1] * grid[2]
    chans_in = act.shape[-1]
    cols = grad.shape[-1]
    placed = jnp.pad(
        grad.transpose(3, 0, 1, 2),
        ((0, 0), (0, grid[0] - grad.shape[0]), (0, grid[1] - grad.shape[1]), (0, grid[2] - grad.shape[2])),
    ).reshape(cols, positions)
    plane, row = grid[1] * grid[2], grid[2]
    offsets = [t * plane + r * row + s for t in range(3) for r in range(3) for s in range(3)]
    lead = max(offsets)
    prefixed = jnp.pad(placed, ((0, 0), (lead, 0)))
    taps = jnp.concatenate([prefixed[:, lead - o : lead - o + positions] for o in offsets], axis=0)
    out = lax.dot_general(
        taps,
        padded.reshape(positions, chans_in),
        (((1,), (0,)), ((), ())),
        preferred_element_type=jnp.float32,
    )
    return out.reshape(27, cols, chans_in).transpose(0, 2, 1).reshape(27 * chans_in, cols)


def digits_of(size, radices):
    out, weight = [], 1
    for radix in radices:
        out.append((weight, radix))
        weight *= radix
    assert weight == size
    return out


def gather_frames(block, axis, radices):
    me = lax.axis_index(axis)
    size = lax.axis_size(axis)
    held = block[None]
    for weight, radix in digits_of(size, radices):
        options = [held] + [
            lax.ppermute(held, axis, [(i, i ^ (k * weight)) for i in range(size)])
            for k in range(1, radix)
        ]
        options = jnp.stack(options)
        digit = (me // weight) % radix
        held = jnp.concatenate(
            [lax.dynamic_index_in_dim(options, digit ^ v, axis=0, keepdims=False) for v in range(radix)],
            axis=0,
        )
    return held.reshape((size,) + block.shape)


def reduce_blocks(blocks, axis, radices):
    me = lax.axis_index(axis)
    size = lax.axis_size(axis)
    held = blocks
    for weight, radix in digits_of(size, radices):
        grouped = held.reshape(held.shape[0] // radix, radix, held.shape[1])
        digit = (me // weight) % radix
        total = lax.dynamic_index_in_dim(grouped, digit, axis=1, keepdims=False)
        for k in range(1, radix):
            send = lax.dynamic_index_in_dim(grouped, digit ^ k, axis=1, keepdims=False)
            total = total + lax.ppermute(send, axis, [(i, i ^ (k * weight)) for i in range(size)])
        held = total
    return held[0]


def radices_of(size, first):
    out, rest = [], size
    for radix in first:
        if radix > 1 and rest % radix == 0:
            out.append(radix)
            rest //= radix
    while rest > 1:
        out.append(2)
        rest //= 2
    return out


def body(video, cotangent, conv1_weight, conv2_weight):
    own_frame = video[0]
    grad_own = cotangent[0]
    layout = own_frame.shape
    height, width_px, chans = (layout[1], layout[2], layout[3])
    frames = lax.axis_size("tm")
    me = lax.axis_index("tm")
    cols = chans // frames
    grouping = (-1, GROUPS, chans // GROUPS)

    frame_radices = radices_of(frames, (4, 4))
    clip = gather_frames(own_frame[0], "tm", frame_radices)
    grad_out = gather_frames(grad_own[0], "tm", frame_radices)
    clip_layout = clip.shape

    first_normed, first_scale = normalize(clip.astype(jnp.float32))
    first_act = (first_normed * jax.nn.sigmoid(first_normed)).astype(jnp.bfloat16).reshape(clip_layout)
    hidden = conv_clip(first_act, conv1_weight).astype(jnp.bfloat16)
    second_normed, second_scale = normalize(hidden.astype(jnp.float32))
    second_act = (
        (second_normed * jax.nn.sigmoid(second_normed)).astype(jnp.bfloat16).reshape(clip_layout)
    )
    second_padded = jnp.pad(second_act, ((2, 0), (0, 0), (0, 0), (0, 0)))
    window = lax.dynamic_slice_in_dim(second_padded, me, 3, axis=0)
    mixed = conv_window(window, conv2_weight)
    block_out = (own_frame.astype(jnp.float32) + mixed).astype(jnp.bfloat16)

    grad_second = conv_transposed(grad_out, conv2_weight)
    grad_hidden = norm_backward(grad_second.reshape(grouping), second_normed, second_scale)
    grad_hidden = grad_hidden.astype(jnp.bfloat16).reshape(clip_layout)
    grad_first = conv_transposed(grad_hidden, conv1_weight)
    grad_first_act = norm_backward(grad_first.reshape(grouping), first_normed, first_scale)
    grad_first_act = grad_first_act.reshape(clip_layout)
    grad_video = grad_own.astype(jnp.float32) + lax.dynamic_slice_in_dim(grad_first_act, me, 1, axis=0)

    my_cols = lambda values: lax.dynamic_slice_in_dim(values, me * cols, cols, axis=3)
    grad_w2 = weight_grad(second_act, my_cols(grad_out))
    grad_w1 = weight_grad(first_act, my_cols(grad_hidden))
    parts = lax.axis_size("dp")
    rows = grad_w1.shape[0] // parts
    share = rows * cols
    width = -(-2 * share // 1024) * 1024
    blocks = jnp.concatenate(
        [
            grad_w1.reshape(parts, share),
            grad_w2.reshape(parts, share),
            jnp.zeros((parts, width - 2 * share), jnp.float32),
        ],
        axis=1,
    )
    reduced = reduce_blocks(blocks, "dp", radices_of(parts, ()))
    factor = 1.0 / math.sqrt(frames * parts * height * width_px)
    total_w1 = reduced[:share].reshape(rows, cols) * factor
    total_w2 = reduced[share : 2 * share].reshape(rows, cols) * factor
    return (block_out[None], grad_video[None], total_w1, total_w2)


def solution(mesh):
    placed = (P("dp", "tm", None, None, None), P("dp", "tm", None, None, None), P(), P())
    return jax.shard_map(
        body,
        mesh=mesh,
        in_specs=placed,
        out_specs=(
            P("dp", "tm", None, None, None),
            P("dp", "tm", None, None, None),
            P("dp", "tm"),
            P("dp", "tm"),
        ),
        check_vma=False,
    )
```
